32 devices in a mesh: dp: 8 (over z, x), mp: 4 (over y, core).
Axes of the slice: x: 2, y: 2, z: 4, core: 2. Of those that a mesh axis runs over, the one named last changes fastest.
Arguments:
- tokens: bfloat16 [64, 256, 768], P(('dp', 'mp')), may hold values from -6 to 6
- cotangent: bfloat16 [64, 256, 768], P(('dp', 'mp')), may hold values from -6 to 6
- segment_ids: int32 [64, 256], P('dp'), may hold values from 0 to 32, as said below
- live_mask: int32 [64, 256], P('dp'), may hold values from 0 to 1, as said below
- expert_ids: int32 [64], P('dp'), may hold values from 0 to 1, as said below
- qkv_weight: bfloat16 [768, 3, 768], P(None, None, 'mp'), may hold values from -0.21875 to 0.21875
- out_weight: bfloat16 [768, 768], P('mp'), may hold values from -0.875 to 0.875
- in_weight: bfloat16 [2, 768, 3072], P(None, None, 'mp'), may hold values from -0.21875 to 0.21875
- down_weight: bfloat16 [2, 3072, 768], P(None, 'mp'), may hold values from -0.15625 to 0.15625
- gain_attn: float32 [768], replicated, may hold values from 0.5 to 1.5
- shift_attn: float32 [768], replicated, may hold values from -3 to 3
- gain_ffn: float32 [768], replicated, may hold values from 0.5 to 1.5
- shift_ffn: float32 [768], replicated, may hold values from -3 to 3
Outputs:
- output: bfloat16 [64, 256, 768], P(('dp', 'mp'))
- grad_tokens: float32 [64, 256, 768], P(('dp', 'mp'))
- counts: int32 [2], replicated
- grad_qkv_weight: float32 [768, 3, 768], P(None, None, 'mp')
- grad_out_weight: float32 [768, 768], P('mp')
- grad_in_weight: float32 [2, 768, 3072], P(None, None, 'mp')
- grad_down_weight: float32 [2, 3072, 768], P(None, 'mp')
- grad_gain_attn: float32 [768], replicated
- grad_shift_attn: float32 [768], replicated
- grad_gain_ffn: float32 [768], replicated
- grad_shift_ffn: float32 [768], replicated
The draws below stay inside these ranges and needn't reach their ends.
Inputs may be any that keep to these rules, and one draw needn't show every extreme that they name: `segment_ids`: ids never fall along a row; the live slots with one id form one caption of 8 to 40 tokens, and captions of both lengths occur; padding slots carry the id 32. `live_mask`: each row is 1 on its first live slots and 0 on the padding after them; every row has live slots. `expert_ids`: every expert is named by some row.
All inputs are finite; a program needn't handle non-finite values.
Results may differ from the reference program's by a relative error of at most 0.018.
Values may be sent and summed in bfloat16 or wider, within the bound.
No kernel may reach another device: no remote copies, remote signals or barrier semaphores. Data moves between devices by JAX's collectives and lax.ppermute only.
A program may use at most 128 MiB of HBM per device.

```python
from functools import partial
import jax
import jax.numpy as jnp
from jax import lax

D = 768
HEADS = 12
HD = 64
FF = 3072
EXPERTS = 2
SLOTS = 256
CAPS = 32
CAP_MIN = 8
CAP_MAX = 40
ROWS_DEV = 8
ROWS = 64


def caption_layout(key):
    lengths = jax.random.randint(jax.random.fold_in(key, 11), (ROWS, CAPS), CAP_MIN, CAP_MAX + 1)
    lengths = lengths.at[0, 0].set(CAP_MAX).at[0, 1].set(CAP_MIN)
    caption_ends = jnp.cumsum(lengths, axis=1)
    row_index = jnp.arange(ROWS)
    floor_live = SLOTS * 5 // 16
    live_limit = floor_live + (SLOTS - floor_live) * row_index // max(ROWS - 1, 1)
    fitting = jnp.where(caption_ends <= live_limit[:, None], caption_ends, 0)
    live_length = jnp.max(fitting, axis=1)
    slot_index = jnp.arange(SLOTS)
    live_slots = (slot_index[None, :] < live_length[:, None]).astype(jnp.int32)
    caption = jnp.sum((caption_ends[:, None, :] <= slot_index[None, :, None]).astype(jnp.int32), axis=2)
    segment = jnp.where(live_slots == 1, caption, CAPS).astype(jnp.int32)
    return (segment, live_slots)


def draw_segment_ids(key, part):
    return caption_layout(key)[0]


def draw_live_mask(key, part):
    return caption_layout(key)[1]


def draw_expert_ids(key, part):
    chosen = jax.random.randint(jax.random.fold_in(key, 23), (ROWS,), 0, EXPERTS)
    return chosen.at[0].set(0).at[1].set(1).astype(jnp.int32)


def level_of(stream_key, extent, split, least, high):
    gain = 1.0
    for axis_at, parts in split:
        draws = jax.random.uniform(jax.random.fold_in(jax.random.fold_in(stream_key, 6), axis_at), (parts,), jnp.float32, least / len(split), high / len(split))
        gain = gain * jnp.repeat(jnp.exp(draws), extent[axis_at] // parts).reshape((-1,) + (1,) * (len(extent) - 1 - axis_at))
    return gain


def normal_values(own_key, extent, width, bound, shards=(), held_as=jnp.bfloat16):
    values = width * jax.random.normal(own_key, extent, jnp.float32)
    if shards:
        values = values * level_of(own_key, extent, shards, -0.22, 0.18)
    return jnp.clip(values, -bound, bound).astype(held_as)


def setup_inputs(seed: int = 0) -> dict:
    arg_keys = jax.random.split(jax.random.key(seed), 14)
    tokens = normal_values(arg_keys[0], (ROWS, SLOTS, D), 1.0, 6.0, ((0, 32),))
    cotangent = normal_values(arg_keys[1], (ROWS, SLOTS, D), 1.0, 6.0, ((0, 32),))
    segment_ids = draw_segment_ids(jax.random.fold_in(arg_keys[13], 71), 0)
    live_mask = draw_live_mask(jax.random.fold_in(arg_keys[13], 71), 0)
    expert_ids = draw_expert_ids(jax.random.fold_in(arg_keys[13], 71), 0)
    qkv_weight = normal_values(arg_keys[5], (D, 3, HEADS * HD), D ** -0.5, 0.21875, ((2, 4),))
    out_weight = normal_values(arg_keys[6], (HEADS * HD, D), (HEADS * HD // 16) ** -0.5, 0.875, ((0, 4),))
    in_weight = normal_values(arg_keys[7], (EXPERTS, D, FF), D ** -0.5, 0.21875, ((2, 4),))
    down_weight = normal_values(arg_keys[8], (EXPERTS, FF, D), (FF // 2) ** -0.5, 0.15625, ((1, 4),))
    gain_attn = jnp.clip(1.0 + 0.1 * jax.random.normal(arg_keys[9], (D,), jnp.float32), 0.5, 1.5)
    shift_attn = normal_values(arg_keys[10], (D,), 0.3, 3.0, (), jnp.float32)
    gain_ffn = jnp.clip(1.0 + 0.1 * jax.random.normal(arg_keys[11], (D,), jnp.float32), 0.5, 1.5)
    shift_ffn = normal_values(arg_keys[12], (D,), 0.3, 3.0, (), jnp.float32)
    return dict(tokens=tokens, cotangent=cotangent, segment_ids=segment_ids, live_mask=live_mask, expert_ids=expert_ids, qkv_weight=qkv_weight, out_weight=out_weight, in_weight=in_weight, down_weight=down_weight, gain_attn=gain_attn, shift_attn=shift_attn, gain_ffn=gain_ffn, shift_ffn=shift_ffn)


@jax.custom_vjp
def low(v):
    return lax.optimization_barrier(v.astype(jnp.bfloat16)).astype(jnp.float32)

@jax.custom_vjp
def low_back(v):
    return v

def low_keep(v):
    return (low(v), None)

def low_pass(kept, grad):
    return (grad,)

def back_keep(v):
    return (v, None)

def back_low(kept, grad):
    return (low(grad),)
low.defvjp(low_keep, low_pass)
low_back.defvjp(back_keep, back_low)
norm_epsilon = 1e-05
masked_fill = -1e+30
highest = lax.Precision.HIGHEST

def layer_norm(values, norm_gain, norm_shift):
    average = lax.optimization_barrier(jnp.mean(values, axis=-1, keepdims=True))
    centred = values - average
    variance = lax.optimization_barrier(jnp.mean(centred * centred, axis=-1, keepdims=True))
    return centred * lax.rsqrt(variance + norm_epsilon) * norm_gain + norm_shift

def group_forward(param_vals, token_vals, seg_vals, live_vals, hot_vals):
    qkv_matrix, out_matrix, in_matrix, down_matrix, attn_gain, attn_shift, ffn_gain, ffn_shift = param_vals
    group_rows = token_vals.shape[0]
    score_scale = HD ** (-0.5)
    normed_one = low(layer_norm(token_vals, attn_gain, attn_shift))
    qkv_all = jnp.einsum('bsd,dk->bsk', normed_one, qkv_matrix.reshape(D, 3 * HEADS * HD), precision=highest)
    qkv_all = low(qkv_all).reshape(group_rows, SLOTS, 3, HEADS, HD)
    queries = low_back(qkv_all[:, :, 0])
    key_part = low_back(qkv_all[:, :, 1])
    value_part = low_back(qkv_all[:, :, 2])
    scores = jnp.einsum('bqhd,bkhd->bhqk', queries, key_part, precision=highest) * score_scale
    scores = low_back(scores)
    same_caption = seg_vals[:, :, None] == seg_vals[:, None, :]
    diagonal = jnp.arange(SLOTS)[:, None] == jnp.arange(SLOTS)[None, :]
    allowed = same_caption & ((live_vals[:, None, :] == 1) | diagonal[None])
    masked = jnp.where(allowed[:, None], scores, masked_fill)
    row_top = lax.optimization_barrier(jnp.max(masked, axis=-1, keepdims=True))
    exp_scores = jnp.exp(masked - row_top)
    attn_probs = exp_scores / lax.optimization_barrier(jnp.sum(exp_scores, axis=-1, keepdims=True))
    head_mix = jnp.einsum('bhqk,bkhd->bqhd', low(attn_probs), value_part, precision=highest)
    head_mix = low_back(low(head_mix.reshape(group_rows, SLOTS, HEADS * HD)))
    attn_out = low_back(jnp.einsum('bsk,kd->bsd', head_mix, out_matrix, precision=highest))
    residual = token_vals + attn_out
    normed_two = low(layer_norm(residual, ffn_gain, ffn_shift))
    hot_float = hot_vals.astype(jnp.float32)
    in_rows = jnp.einsum('be,edf->bdf', hot_float, in_matrix, precision=highest)
    upward = low_back(jnp.einsum('bsd,bdf->bsf', normed_two, in_rows, precision=highest))
    activated = low(jax.nn.gelu(upward, approximate=False))
    down_rows = jnp.einsum('be,efd->bfd', hot_float, down_matrix, precision=highest)
    ffn_out = low_back(jnp.einsum('bsf,bfd->bsd', activated, down_rows, precision=highest))
    return residual + ffn_out

def reference(tokens, cotangent, segment_ids, live_mask, expert_ids, qkv_weight, out_weight, in_weight, down_weight, gain_attn, shift_attn, gain_ffn, shift_ffn):
    expert_hot = expert_ids[:, None] == jnp.arange(EXPERTS)[None, :]
    row_live = lax.optimization_barrier(jnp.sum(live_mask, axis=1))
    counts = lax.optimization_barrier(jnp.sum(jnp.where(expert_hot, row_live[:, None], 0), axis=0)).astype(jnp.int32)
    count_float = counts.astype(jnp.float32)
    loss_weight = jnp.sum(count_float) / (EXPERTS * count_float)
    row_weight = lax.optimization_barrier(jnp.sum(jnp.where(expert_hot, loss_weight[None, :], 0.0), axis=1))
    grad_output = cotangent.astype(jnp.float32) * live_mask[:, :, None].astype(jnp.float32) * row_weight[:, None, None]
    params = (qkv_weight.astype(jnp.float32), out_weight.astype(jnp.float32), in_weight.astype(jnp.float32), down_weight.astype(jnp.float32), gain_attn.astype(jnp.float32), shift_attn.astype(jnp.float32), gain_ffn.astype(jnp.float32), shift_ffn.astype(jnp.float32))
    groups = ROWS // ROWS_DEV

    def forward(token_vals, *param_vals):
        block = jax.checkpoint(partial(group_forward, param_vals))

        def run_group(pieces):
            return block(pieces[0], pieces[1], pieces[2], pieces[3])
        stacked = lax.map(run_group, (token_vals.reshape(groups, ROWS_DEV, SLOTS, D), segment_ids.reshape(groups, ROWS_DEV, SLOTS), live_mask.reshape(groups, ROWS_DEV, SLOTS), expert_hot.reshape(groups, ROWS_DEV, EXPERTS)))
        return stacked.reshape(ROWS, SLOTS, D)
    result, backward = jax.vjp(forward, tokens.astype(jnp.float32), *params)
    grads = backward(grad_output)
    return (result.astype(jnp.bfloat16), grads[0], counts, grads[1], grads[2], grads[3], grads[4], grads[5], grads[6], grads[7], grads[8])
```

```python
import jax
import jax.numpy as jnp
from jax import lax
from jax.sharding import PartitionSpec as P

HD = 64


norm_epsilon = 1e-05
masked_fill = -1e30


def layer_norm(values, norm_gain, norm_shift):
    average = jnp.mean(values, axis=-1, keepdims=True)
    centred = values - average
    variance = jnp.mean(centred * centred, axis=-1, keepdims=True)
    return centred * lax.rsqrt(variance + norm_epsilon) * norm_gain + norm_shift


def gelu_exact(values):
    return jax.nn.gelu(values, approximate=False)


def select_rows(values, hot_column):
    return values * hot_column[:, None, None]


def per_device(
    tokens,
    cotangent,
    segment_ids,
    live_mask,
    expert_ids,
    qkv_weight,
    out_weight,
    in_weight,
    down_weight,
    gain_attn,
    shift_attn,
    gain_ffn,
    shift_ffn,
):
    local_rows, slots, model_width = tokens.shape
    experts = in_weight.shape[0]
    heads_local = qkv_weight.shape[2] // HD
    score_scale = HD ** (-0.5)
    first_row = lax.axis_index("mp") * local_rows
    expert_hot = expert_ids[:, None] == jnp.arange(experts)[None, :]
    row_live = jnp.sum(live_mask, axis=1)
    local_counts = jnp.sum(jnp.where(expert_hot, row_live[:, None], 0), axis=0)
    counts = lax.psum(local_counts, "dp")
    hot_matrix = expert_hot.astype(jnp.bfloat16)
    token_float = tokens.astype(jnp.float32)
    norm_one = layer_norm(token_float, gain_attn, shift_attn).astype(jnp.bfloat16)
    norm_one_full = lax.all_gather(norm_one, "mp", axis=0, tiled=True)
    qkv_flat = qkv_weight.reshape(model_width, -1)
    qkv_all = jnp.einsum(
        "rsd,dk->rsk", norm_one_full, qkv_flat, preferred_element_type=jnp.float32
    ).astype(jnp.bfloat16)
    group_rows = qkv_all.shape[0]
    qkv_split = qkv_all.reshape(group_rows, slots, 3, heads_local, HD)
    queries = qkv_split[:, :, 0]
    key_part = qkv_split[:, :, 1]
    value_part = qkv_split[:, :, 2]
    same_caption = segment_ids[:, :, None] == segment_ids[:, None, :]
    diagonal = jnp.arange(slots)[:, None] == jnp.arange(slots)[None, :]
    allowed = (same_caption & ((live_mask[:, None, :] == 1) | diagonal[None]))[:, None]

    def masked_scores():
        raw_scores = (
            jnp.einsum("rqhd,rkhd->rhqk", queries, key_part, preferred_element_type=jnp.float32)
            * score_scale
        )
        return jnp.where(allowed, raw_scores, masked_fill)

    scores = masked_scores()
    row_top = jnp.max(scores, axis=-1, keepdims=True)
    exp_scores = jnp.exp(scores - row_top)
    row_total = jnp.sum(exp_scores, axis=-1, keepdims=True)
    attn_probs = exp_scores / row_total
    log_total = row_top + jnp.log(row_total)
    head_mix = jnp.einsum(
        "rhqk,rkhd->rqhd",
        attn_probs.astype(jnp.bfloat16),
        value_part,
        preferred_element_type=jnp.float32,
    )
    head_mix = head_mix.reshape(group_rows, slots, heads_local * HD).astype(jnp.bfloat16)
    picked = head_mix
    attn_local = lax.psum_scatter(
        jnp.einsum("rsk,kd->rsd", picked, out_weight, preferred_element_type=jnp.float32).astype(
            jnp.bfloat16
        ),
        "mp",
        scatter_dimension=0,
        tiled=True,
    ).astype(jnp.float32)
    residual = token_float + attn_local
    norm_two = layer_norm(residual, gain_ffn, shift_ffn).astype(jnp.bfloat16)
    norm_two_full = lax.all_gather(norm_two, "mp", axis=0, tiled=True)
    upward = jnp.zeros((group_rows, slots, in_weight.shape[2]), jnp.float32)
    for expert in range(experts):
        upward = upward + jnp.einsum(
            "rsd,df->rsf",
            select_rows(norm_two_full, hot_matrix[:, expert]),
            in_weight[expert],
            preferred_element_type=jnp.float32,
        )
    activated = gelu_exact(upward).astype(jnp.bfloat16)
    picked = activated
    hot_picked = hot_matrix
    total = jnp.zeros((local_rows * lax.axis_size("mp"), slots, model_width), jnp.float32)
    for ffn_expert in range(experts):
        total = total + jnp.einsum(
            "rsf,fd->rsd",
            select_rows(picked, hot_picked[:, ffn_expert]),
            down_weight[ffn_expert],
            preferred_element_type=jnp.float32,
        )
    ffn_local = lax.psum_scatter(
        total.astype(jnp.bfloat16), "mp", scatter_dimension=0, tiled=True
    ).astype(jnp.float32)
    output = (residual + ffn_local).astype(jnp.bfloat16)
    count_float = counts.astype(jnp.float32)
    loss_weight = jnp.sum(count_float) / (experts * count_float)
    local_hot = lax.dynamic_slice_in_dim(expert_hot, first_row, local_rows, 0)
    row_weight = jnp.sum(jnp.where(local_hot, loss_weight[None, :], 0.0), axis=1)
    live_local = lax.dynamic_slice_in_dim(live_mask, first_row, local_rows, 0)
    grad_output = (
        cotangent.astype(jnp.float32)
        * live_local[:, :, None].astype(jnp.float32)
        * row_weight[:, None, None]
    )
    grad_ffn_full = lax.all_gather(grad_output.astype(jnp.bfloat16), "mp", axis=0, tiled=True)
    grad_act = jnp.zeros(upward.shape, jnp.float32)
    down_list = []
    for expert in range(experts):
        masked_grad = select_rows(grad_ffn_full, hot_matrix[:, expert])
        grad_act = grad_act + jnp.einsum(
            "rsd,fd->rsf", masked_grad, down_weight[expert], preferred_element_type=jnp.float32
        )
        down_list.append(
            jnp.einsum("rsf,rsd->fd", activated, masked_grad, preferred_element_type=jnp.float32)
        )
    grad_down_weight = jnp.stack(down_list, axis=0)
    grad_up = jax.vjp(gelu_exact, upward)[1](grad_act)[0].astype(jnp.bfloat16)
    in_list = []
    for expert in range(experts):
        in_list.append(
            jnp.einsum(
                "rsd,rsf->df",
                select_rows(norm_two_full, hot_matrix[:, expert]),
                grad_up,
                preferred_element_type=jnp.float32,
            )
        )
    grad_in_weight = jnp.stack(in_list, axis=0)
    picked = grad_up
    hot_picked = hot_matrix
    total = jnp.zeros((local_rows * lax.axis_size("mp"), slots, model_width), jnp.float32)
    for expert in range(experts):
        total = total + jnp.einsum(
            "rsf,df->rsd",
            select_rows(picked, hot_picked[:, expert]),
            in_weight[expert],
            preferred_element_type=jnp.float32,
        )
    grad_norm_two = lax.psum_scatter(
        total.astype(jnp.bfloat16), "mp", scatter_dimension=0, tiled=True
    ).astype(jnp.float32)
    second_back = jax.vjp(layer_norm, residual, gain_ffn, shift_ffn)[1]
    grad_from_second, grad_gain_ffn, grad_shift_ffn = second_back(grad_norm_two)
    grad_residual = grad_output + grad_from_second
    grad_attn_full = lax.all_gather(grad_residual.astype(jnp.bfloat16), "mp", axis=0, tiled=True)
    grad_out_weight = jnp.einsum(
        "rsk,rsd->kd", head_mix, grad_attn_full, preferred_element_type=jnp.float32
    )
    grad_mix = jnp.einsum(
        "rsd,kd->rsk", grad_attn_full, out_weight, preferred_element_type=jnp.float32
    )
    grad_mix = grad_mix.astype(jnp.bfloat16).reshape(group_rows, slots, heads_local, HD)
    attn_again = jnp.exp(masked_scores() - log_total)
    grad_probs = jnp.einsum(
        "rqhd,rkhd->rhqk", grad_mix, value_part, preferred_element_type=jnp.float32
    )
    grad_scores = attn_again * (
        grad_probs - jnp.sum(grad_probs * attn_again, axis=-1, keepdims=True)
    )
    grad_scores = grad_scores.astype(jnp.bfloat16)
    grad_value = jnp.einsum(
        "rhqk,rqhd->rkhd",
        attn_again.astype(jnp.bfloat16),
        grad_mix,
        preferred_element_type=jnp.float32,
    )
    grad_query = (
        jnp.einsum("rhqk,rkhd->rqhd", grad_scores, key_part, preferred_element_type=jnp.float32)
        * score_scale
    )
    grad_key = (
        jnp.einsum("rhqk,rqhd->rkhd", grad_scores, queries, preferred_element_type=jnp.float32)
        * score_scale
    )
    grad_qkv = (
        jnp.stack([grad_query, grad_key, grad_value], axis=2)
        .astype(jnp.bfloat16)
        .reshape(group_rows, slots, -1)
    )
    grad_qkv_weight = jnp.einsum(
        "rsd,rsk->dk", norm_one_full, grad_qkv, preferred_element_type=jnp.float32
    )
    grad_qkv_weight = grad_qkv_weight.reshape(qkv_weight.shape)
    picked = grad_qkv
    grad_norm_one = lax.psum_scatter(
        jnp.einsum("rsk,dk->rsd", picked, qkv_flat, preferred_element_type=jnp.float32).astype(
            jnp.bfloat16
        ),
        "mp",
        scatter_dimension=0,
        tiled=True,
    ).astype(jnp.float32)
    first_back = jax.vjp(layer_norm, token_float, gain_attn, shift_attn)[1]
    grad_from_first, grad_gain_attn, grad_shift_attn = first_back(grad_norm_one)
    grad_tokens = grad_residual + grad_from_first
    norm_grads = lax.psum(
        (grad_gain_attn, grad_shift_attn, grad_gain_ffn, grad_shift_ffn), ("dp", "mp")
    )
    summed = lax.psum(
        tuple(
            g.astype(jnp.bfloat16)
            for g in (grad_qkv_weight, grad_out_weight, grad_in_weight, grad_down_weight)
        ),
        "dp",
    )
    summed = tuple(g.astype(jnp.float32) for g in summed)
    return (
        output,
        grad_tokens,
        counts,
        summed[0],
        summed[1],
        summed[2],
        summed[3],
        norm_grads[0],
        norm_grads[1],
        norm_grads[2],
        norm_grads[3],
    )


def solution(mesh):
    in_specs = (
        P(("dp", "mp"), None, None),
        P(("dp", "mp"), None, None),
        P("dp", None),
        P("dp", None),
        P("dp"),
        P(None, None, "mp"),
        P("mp", None),
        P(None, None, "mp"),
        P(None, "mp", None),
        P(),
        P(),
        P(),
        P(),
    )
    out_specs = (
        P(("dp", "mp"), None, None),
        P(("dp", "mp"), None, None),
        P(),
        P(None, None, "mp"),
        P("mp", None),
        P(None, None, "mp"),
        P(None, "mp", None),
        P(),
        P(),
        P(),
        P(),
    )
    return jax.shard_map(
        per_device, mesh=mesh, in_specs=in_specs, out_specs=out_specs, check_vma=False
    )
```

```python
import jax
import jax.numpy as jnp
from jax import lax
from jax.sharding import PartitionSpec as P

HD = 64


norm_epsilon = 1e-05
masked_fill = -1e30


def layer_norm(values, norm_gain, norm_shift):
    average = jnp.mean(values, axis=-1, keepdims=True)
    centred = values - average
    variance = jnp.mean(centred * centred, axis=-1, keepdims=True)
    return centred * lax.rsqrt(variance + norm_epsilon) * norm_gain + norm_shift


def gelu_exact(values):
    return jax.nn.gelu(values, approximate=False)


def xor_pairs(size, bit):
    return [(i, i ^ bit) for i in range(size)]


def gather_rows_mp(values):
    if lax.axis_size("mp") != 4:
        return lax.all_gather(values, "mp", axis=0, tiled=True)
    index = lax.axis_index("mp")
    chip_y = index // 2
    core = index % 2
    other_y = lax.ppermute(values, "mp", xor_pairs(4, 2))
    pair = jnp.where(
        chip_y == 0, jnp.stack([values, other_y]), jnp.stack([other_y, values])
    )
    other_core = lax.ppermute(pair, "mp", xor_pairs(4, 1))
    quad = jnp.where(
        core == 0, jnp.stack([pair, other_core], axis=1), jnp.stack([other_core, pair], axis=1)
    )
    return quad.reshape((-1,) + values.shape[1:])


def scatter_rows_mp(partial):
    if lax.axis_size("mp") != 4:
        return lax.psum_scatter(
            partial.astype(jnp.bfloat16), "mp", scatter_dimension=0, tiled=True
        ).astype(jnp.float32)
    index = lax.axis_index("mp")
    chip_y = index // 2
    core = index % 2
    rows = partial.shape[0] // 4
    blocks = partial.reshape((2, 2, rows) + partial.shape[1:])
    keep = lax.dynamic_index_in_dim(blocks, core, axis=1, keepdims=False)
    send = lax.dynamic_index_in_dim(blocks, 1 - core, axis=1, keepdims=False)
    got = lax.ppermute(send.astype(jnp.bfloat16), "mp", xor_pairs(4, 1))
    chip_sum = keep + got.astype(jnp.float32)
    keep_y = lax.dynamic_index_in_dim(chip_sum, chip_y, axis=0, keepdims=False)
    send_y = lax.dynamic_index_in_dim(chip_sum, 1 - chip_y, axis=0, keepdims=False)
    got_y = lax.ppermute(send_y.astype(jnp.bfloat16), "mp", xor_pairs(4, 2))
    return keep_y + got_y.astype(jnp.float32)


def butterfly_sum(values, axis):
    size = lax.axis_size(axis)
    if size & (size - 1):
        return lax.psum(values, axis)
    bit = 1
    while bit < size:
        values = jax.tree.map(
            lambda v: v + lax.ppermute(v, axis, xor_pairs(size, bit)), values
        )
        bit *= 2
    return values


def select_rows(values, hot_column):
    return values * hot_column[:, None, None]


def per_device(
    tokens,
    cotangent,
    segment_ids,
    live_mask,
    expert_ids,
    qkv_weight,
    out_weight,
    in_weight,
    down_weight,
    gain_attn,
    shift_attn,
    gain_ffn,
    shift_ffn,
):
    local_rows, slots, model_width = tokens.shape
    experts = in_weight.shape[0]
    heads_local = qkv_weight.shape[2] // HD
    score_scale = HD ** (-0.5)
    first_row = lax.axis_index("mp") * local_rows
    expert_hot = expert_ids[:, None] == jnp.arange(experts)[None, :]
    row_live = jnp.sum(live_mask, axis=1)
    local_counts = jnp.sum(jnp.where(expert_hot, row_live[:, None], 0), axis=0)
    counts = butterfly_sum(local_counts, "dp")
    hot_matrix = expert_hot.astype(jnp.bfloat16)
    token_float = tokens.astype(jnp.float32)
    norm_one = layer_norm(token_float, gain_attn, shift_attn).astype(jnp.bfloat16)
    norm_one_full = gather_rows_mp(norm_one)
    qkv_flat = qkv_weight.reshape(model_width, -1)
    qkv_all = jnp.einsum(
        "rsd,dk->rsk", norm_one_full, qkv_flat, preferred_element_type=jnp.float32
    ).astype(jnp.bfloat16)
    group_rows = qkv_all.shape[0]
    qkv_split = qkv_all.reshape(group_rows, slots, 3, heads_local, HD)
    queries = qkv_split[:, :, 0]
    key_part = qkv_split[:, :, 1]
    value_part = qkv_split[:, :, 2]
    same_caption = segment_ids[:, :, None] == segment_ids[:, None, :]
    diagonal = jnp.arange(slots)[:, None] == jnp.arange(slots)[None, :]
    allowed = (same_caption & ((live_mask[:, None, :] == 1) | diagonal[None]))[:, None]

    def masked_scores():
        raw_scores = (
            jnp.einsum("rqhd,rkhd->rhqk", queries, key_part, preferred_element_type=jnp.float32)
            * score_scale
        )
        return jnp.where(allowed, raw_scores, masked_fill)

    scores = masked_scores()
    row_top = jnp.max(scores, axis=-1, keepdims=True)
    exp_scores = jnp.exp(scores - row_top)
    row_total = jnp.sum(exp_scores, axis=-1, keepdims=True)
    attn_probs = exp_scores / row_total
    log_total = row_top + jnp.log(row_total)
    head_mix = jnp.einsum(
        "rhqk,rkhd->rqhd",
        attn_probs.astype(jnp.bfloat16),
        value_part,
        preferred_element_type=jnp.float32,
    )
    head_mix = head_mix.reshape(group_rows, slots, heads_local * HD).astype(jnp.bfloat16)
    picked = head_mix
    attn_local = scatter_rows_mp(
        jnp.einsum("rsk,kd->rsd", picked, out_weight, preferred_element_type=jnp.float32)
    )
    residual = token_float + attn_local
    norm_two = layer_norm(residual, gain_ffn, shift_ffn).astype(jnp.bfloat16)
    norm_two_full = gather_rows_mp(norm_two)
    upward = jnp.zeros((group_rows, slots, in_weight.shape[2]), jnp.float32)
    for expert in range(experts):
        upward = upward + jnp.einsum(
            "rsd,df->rsf",
            select_rows(norm_two_full, hot_matrix[:, expert]),
            in_weight[expert],
            preferred_element_type=jnp.float32,
        )
    activated = gelu_exact(upward).astype(jnp.bfloat16)
    picked = activated
    hot_picked = hot_matrix
    total = jnp.zeros((local_rows * lax.axis_size("mp"), slots, model_width), jnp.float32)
    for ffn_expert in range(experts):
        total = total + jnp.einsum(
            "rsf,fd->rsd",
            select_rows(picked, hot_picked[:, ffn_expert]),
            down_weight[ffn_expert],
            preferred_element_type=jnp.float32,
        )
    ffn_local = scatter_rows_mp(total)
    output = (residual + ffn_local).astype(jnp.bfloat16)
    count_float = counts.astype(jnp.float32)
    loss_weight = jnp.sum(count_float) / (experts * count_float)
    local_hot = lax.dynamic_slice_in_dim(expert_hot, first_row, local_rows, 0)
    row_weight = jnp.sum(jnp.where(local_hot, loss_weight[None, :], 0.0), axis=1)
    live_local = lax.dynamic_slice_in_dim(live_mask, first_row, local_rows, 0)
    grad_output = (
        cotangent.astype(jnp.float32)
        * live_local[:, :, None].astype(jnp.float32)
        * row_weight[:, None, None]
    )
    grad_ffn_full = gather_rows_mp(grad_output.astype(jnp.bfloat16))
    grad_act = jnp.zeros(upward.shape, jnp.float32)
    down_list = []
    for expert in range(experts):
        masked_grad = select_rows(grad_ffn_full, hot_matrix[:, expert])
        grad_act = grad_act + jnp.einsum(
            "rsd,fd->rsf", masked_grad, down_weight[expert], preferred_element_type=jnp.float32
        )
        down_list.append(
            jnp.einsum("rsf,rsd->fd", activated, masked_grad, preferred_element_type=jnp.float32)
        )
    grad_down_weight = jnp.stack(down_list, axis=0)
    grad_up = jax.vjp(gelu_exact, upward)[1](grad_act)[0].astype(jnp.bfloat16)
    in_list = []
    for expert in range(experts):
        in_list.append(
            jnp.einsum(
                "rsd,rsf->df",
                select_rows(norm_two_full, hot_matrix[:, expert]),
                grad_up,
                preferred_element_type=jnp.float32,
            )
        )
    grad_in_weight = jnp.stack(in_list, axis=0)
    ffn_grads = (grad_in_weight.astype(jnp.bfloat16), grad_down_weight.astype(jnp.bfloat16))
    picked = grad_up
    hot_picked = hot_matrix
    total = jnp.zeros((local_rows * lax.axis_size("mp"), slots, model_width), jnp.float32)
    for expert in range(experts):
        total = total + jnp.einsum(
            "rsf,df->rsd",
            select_rows(picked, hot_picked[:, expert]),
            in_weight[expert],
            preferred_element_type=jnp.float32,
        )
    grad_norm_two = scatter_rows_mp(total)
    second_back = jax.vjp(layer_norm, residual, gain_ffn, shift_ffn)[1]
    grad_from_second, grad_gain_ffn, grad_shift_ffn = second_back(grad_norm_two)
    grad_residual = grad_output + grad_from_second
    ffn_grads, grad_residual = lax.optimization_barrier((ffn_grads, grad_residual))
    ffn_summed = lax.psum(ffn_grads, "dp")
    grad_attn_full = gather_rows_mp(grad_residual.astype(jnp.bfloat16))
    grad_out_weight = jnp.einsum(
        "rsk,rsd->kd", head_mix, grad_attn_full, preferred_element_type=jnp.float32
    )
    grad_mix = jnp.einsum(
        "rsd,kd->rsk", grad_attn_full, out_weight, preferred_element_type=jnp.float32
    )
    grad_mix = grad_mix.astype(jnp.bfloat16).reshape(group_rows, slots, heads_local, HD)
    attn_again = jnp.exp(masked_scores() - log_total)
    grad_probs = jnp.einsum(
        "rqhd,rkhd->rhqk", grad_mix, value_part, preferred_element_type=jnp.float32
    )
    grad_scores = attn_again * (
        grad_probs - jnp.sum(grad_probs * attn_again, axis=-1, keepdims=True)
    )
    grad_scores = grad_scores.astype(jnp.bfloat16)
    grad_value = jnp.einsum(
        "rhqk,rqhd->rkhd",
        attn_again.astype(jnp.bfloat16),
        grad_mix,
        preferred_element_type=jnp.float32,
    )
    grad_query = (
        jnp.einsum("rhqk,rkhd->rqhd", grad_scores, key_part, preferred_element_type=jnp.float32)
        * score_scale
    )
    grad_key = (
        jnp.einsum("rhqk,rqhd->rkhd", grad_scores, queries, preferred_element_type=jnp.float32)
        * score_scale
    )
    grad_qkv = (
        jnp.stack([grad_query, grad_key, grad_value], axis=2)
        .astype(jnp.bfloat16)
        .reshape(group_rows, slots, -1)
    )
    grad_qkv_weight = jnp.einsum(
        "rsd,rsk->dk", norm_one_full, grad_qkv, preferred_element_type=jnp.float32
    )
    grad_qkv_weight = grad_qkv_weight.reshape(qkv_weight.shape)
    picked = grad_qkv
    grad_norm_one = scatter_rows_mp(
        jnp.einsum("rsk,dk->rsd", picked, qkv_flat, preferred_element_type=jnp.float32)
    )
    first_back = jax.vjp(layer_norm, token_float, gain_attn, shift_attn)[1]
    grad_from_first, grad_gain_attn, grad_shift_attn = first_back(grad_norm_one)
    grad_tokens = grad_residual + grad_from_first
    norm_grads = butterfly_sum(
        butterfly_sum(
            jnp.stack([grad_gain_attn, grad_shift_attn, grad_gain_ffn, grad_shift_ffn]), "mp"
        ),
        "dp",
    )
    attn_grads, ffn_summed = lax.optimization_barrier(
        ((grad_qkv_weight.astype(jnp.bfloat16), grad_out_weight.astype(jnp.bfloat16)), ffn_summed)
    )
    attn_summed = lax.psum(attn_grads, "dp")
    summed = tuple(g.astype(jnp.float32) for g in attn_summed + ffn_summed)
    return (
        output,
        grad_tokens,
        counts,
        summed[0],
        summed[1],
        summed[2],
        summed[3],
        norm_grads[0],
        norm_grads[1],
        norm_grads[2],
        norm_grads[3],
    )


def solution(mesh):
    in_specs = (
        P(("dp", "mp"), None, None),
        P(("dp", "mp"), None, None),
        P("dp", None),
        P("dp", None),
        P("dp"),
        P(None, None, "mp"),
        P("mp", None),
        P(None, None, "mp"),
        P(None, "mp", None),
        P(),
        P(),
        P(),
        P(),
    )
    out_specs = (
        P(("dp", "mp"), None, None),
        P(("dp", "mp"), None, None),
        P(),
        P(None, None, "mp"),
        P("mp", None),
        P(None, None, "mp"),
        P(None, "mp", None),
        P(),
        P(),
        P(),
        P(),
    )
    return jax.shard_map(
        per_device, mesh=mesh, in_specs=in_specs, out_specs=out_specs, check_vma=False
    )
```

```python
import jax
import jax.numpy as jnp
from jax import lax
from jax.sharding import PartitionSpec as P


HD = 64


norm_epsilon = 1e-05
masked_fill = -1e30


def layer_norm(values, norm_gain, norm_shift):
    average = jnp.mean(values, axis=-1, keepdims=True)
    centred = values - average
    variance = jnp.mean(centred * centred, axis=-1, keepdims=True)
    return centred * lax.rsqrt(variance + norm_epsilon) * norm_gain + norm_shift


def gelu_exact(values):
    return jax.nn.gelu(values, approximate=False)


def xor_pairs(size, bit):
    return [(i, i ^ bit) for i in range(size)]


def gather_rows_mp(values):
    if lax.axis_size("mp") != 4:
        return lax.all_gather(values, "mp", axis=0, tiled=True)
    index = lax.axis_index("mp")
    chip_y = index // 2
    core = index % 2
    other_y = lax.ppermute(values, "mp", xor_pairs(4, 2))
    pair = jnp.where(
        chip_y == 0, jnp.stack([values, other_y]), jnp.stack([other_y, values])
    )
    other_core = lax.ppermute(pair, "mp", xor_pairs(4, 1))
    quad = jnp.where(
        core == 0, jnp.stack([pair, other_core], axis=1), jnp.stack([other_core, pair], axis=1)
    )
    return quad.reshape((-1,) + values.shape[1:])


def scatter_rows_mp(partial, tie=None):
    if lax.axis_size("mp") != 4:
        result = lax.psum_scatter(
            partial.astype(jnp.bfloat16), "mp", scatter_dimension=0, tiled=True
        ).astype(jnp.float32)
        return result if tie is None else (result, tie)
    index = lax.axis_index("mp")
    chip_y = index // 2
    core = index % 2
    rows = partial.shape[0] // 4
    blocks = partial.reshape((2, 2, rows) + partial.shape[1:])
    keep = lax.dynamic_index_in_dim(blocks, core, axis=1, keepdims=False)
    send = lax.dynamic_index_in_dim(blocks, 1 - core, axis=1, keepdims=False)
    got = lax.ppermute(send.astype(jnp.bfloat16), "mp", xor_pairs(4, 1))
    chip_sum = keep + got.astype(jnp.float32)
    keep_y = lax.dynamic_index_in_dim(chip_sum, chip_y, axis=0, keepdims=False)
    send_y = lax.dynamic_index_in_dim(chip_sum, 1 - chip_y, axis=0, keepdims=False)
    got_y = lax.ppermute(send_y.astype(jnp.bfloat16), "mp", xor_pairs(4, 2))
    if tie is not None:
        tie, got_y = lax.optimization_barrier((tie, got_y))
    result = keep_y + got_y.astype(jnp.float32)
    return result if tie is None else (result, tie)


def butterfly_sum(values, axis):
    size = lax.axis_size(axis)
    if size & (size - 1):
        return lax.psum(values, axis)
    bit = 1
    while bit < size:
        values = jax.tree.map(
            lambda v: v + lax.ppermute(v, axis, xor_pairs(size, bit)), values
        )
        bit *= 2
    return values


def butterfly_allreduce_low(values, axis):
    size = lax.axis_size(axis)
    flat = jnp.concatenate([v.reshape(-1).astype(jnp.float32) for v in values])
    if size & (size - 1) or flat.shape[0] % size:
        summed = lax.psum(flat.astype(jnp.bfloat16), axis)
    else:
        steps = size.bit_length() - 1
        index = lax.axis_index(axis)
        chunk = flat.shape[0] // size
        held = flat.reshape((2,) * steps + (chunk,))
        for step in range(steps):
            bit = 1 << step
            mine = (index // bit) % 2
            last = steps - 1 - step
            keep = lax.dynamic_index_in_dim(held, mine, axis=last, keepdims=False)
            send = lax.dynamic_index_in_dim(held, 1 - mine, axis=last, keepdims=False)
            got = lax.ppermute(send.astype(jnp.bfloat16), axis, xor_pairs(size, bit))
            held = keep + got.astype(jnp.float32)
        held = held.astype(jnp.bfloat16)
        for step in reversed(range(steps)):
            bit = 1 << step
            mine = (index // bit) % 2
            got = lax.ppermute(held, axis, xor_pairs(size, bit))
            place = steps - 1 - step
            held = jnp.where(
                mine == 0, jnp.stack([held, got], axis=place), jnp.stack([got, held], axis=place)
            )
        summed = held.reshape(-1)
    out, start = [], 0
    for v in values:
        out.append(summed[start : start + v.size].reshape(v.shape).astype(jnp.float32))
        start += v.size
    return tuple(out)


def select_rows(values, hot_column):
    return values * hot_column[:, None, None]


def per_device(
    tokens,
    cotangent,
    segment_ids,
    live_mask,
    expert_ids,
    qkv_weight,
    out_weight,
    in_weight,
    down_weight,
    gain_attn,
    shift_attn,
    gain_ffn,
    shift_ffn,
):
    local_rows, slots, model_width = tokens.shape
    experts = in_weight.shape[0]
    heads_local = qkv_weight.shape[2] // HD
    score_scale = HD ** (-0.5)
    first_row = lax.axis_index("mp") * local_rows
    expert_hot = expert_ids[:, None] == jnp.arange(experts)[None, :]
    row_live = jnp.sum(live_mask, axis=1)
    local_counts = jnp.sum(jnp.where(expert_hot, row_live[:, None], 0), axis=0)
    counts = butterfly_sum(local_counts, "dp")
    hot_matrix = expert_hot.astype(jnp.bfloat16)
    token_float = tokens.astype(jnp.float32)
    norm_one = layer_norm(token_float, gain_attn, shift_attn).astype(jnp.bfloat16)
    norm_one_full = gather_rows_mp(norm_one)
    qkv_flat = qkv_weight.reshape(model_width, -1)
    qkv_all = jnp.einsum(
        "rsd,dk->rsk", norm_one_full, qkv_flat, preferred_element_type=jnp.float32
    ).astype(jnp.bfloat16)
    group_rows = qkv_all.shape[0]
    qkv_split = qkv_all.reshape(group_rows, slots, 3, heads_local, HD)
    queries = qkv_split[:, :, 0]
    key_part = qkv_split[:, :, 1]
    value_part = qkv_split[:, :, 2]
    same_caption = segment_ids[:, :, None] == segment_ids[:, None, :]
    diagonal = jnp.arange(slots)[:, None] == jnp.arange(slots)[None, :]
    allowed = (same_caption & ((live_mask[:, None, :] == 1) | diagonal[None]))[:, None]

    def masked_scores():
        raw_scores = (
            jnp.einsum("rqhd,rkhd->rhqk", queries, key_part, preferred_element_type=jnp.float32)
            * score_scale
        )
        return jnp.where(allowed, raw_scores, masked_fill)

    scores = masked_scores()
    row_top = jnp.max(scores, axis=-1, keepdims=True)
    exp_scores = jnp.exp(scores - row_top)
    row_total = jnp.sum(exp_scores, axis=-1, keepdims=True)
    attn_probs = exp_scores / row_total
    log_total = row_top + jnp.log(row_total)
    head_mix = jnp.einsum(
        "rhqk,rkhd->rqhd",
        attn_probs.astype(jnp.bfloat16),
        value_part,
        preferred_element_type=jnp.float32,
    )
    head_mix = head_mix.reshape(group_rows, slots, heads_local * HD).astype(jnp.bfloat16)
    picked = head_mix
    attn_local = scatter_rows_mp(
        jnp.einsum("rsk,kd->rsd", picked, out_weight, preferred_element_type=jnp.float32)
    )
    residual = token_float + attn_local
    norm_two = layer_norm(residual, gain_ffn, shift_ffn).astype(jnp.bfloat16)
    norm_two_full = gather_rows_mp(norm_two)
    upward = jnp.zeros((group_rows, slots, in_weight.shape[2]), jnp.float32)
    for expert in range(experts):
        upward = upward + jnp.einsum(
            "rsd,df->rsf",
            select_rows(norm_two_full, hot_matrix[:, expert]),
            in_weight[expert],
            preferred_element_type=jnp.float32,
        )
    activated = gelu_exact(upward).astype(jnp.bfloat16)
    picked = activated
    hot_picked = hot_matrix
    total = jnp.zeros((local_rows * lax.axis_size("mp"), slots, model_width), jnp.float32)
    for ffn_expert in range(experts):
        total = total + jnp.einsum(
            "rsf,fd->rsd",
            select_rows(picked, hot_picked[:, ffn_expert]),
            down_weight[ffn_expert],
            preferred_element_type=jnp.float32,
        )
    ffn_partial = total
    count_float = counts.astype(jnp.float32)
    loss_weight = jnp.sum(count_float) / (experts * count_float)
    local_hot = lax.dynamic_slice_in_dim(expert_hot, first_row, local_rows, 0)
    row_weight = jnp.sum(jnp.where(local_hot, loss_weight[None, :], 0.0), axis=1)
    live_local = lax.dynamic_slice_in_dim(live_mask, first_row, local_rows, 0)
    grad_output = (
        cotangent.astype(jnp.float32)
        * live_local[:, :, None].astype(jnp.float32)
        * row_weight[:, None, None]
    )
    grad_ffn_full = gather_rows_mp(grad_output.astype(jnp.bfloat16))
    grad_act = jnp.zeros(upward.shape, jnp.float32)
    down_list = []
    for expert in range(experts):
        masked_grad = select_rows(grad_ffn_full, hot_matrix[:, expert])
        grad_act = grad_act + jnp.einsum(
            "rsd,fd->rsf", masked_grad, down_weight[expert], preferred_element_type=jnp.float32
        )
        down_list.append(
            jnp.einsum("rsf,rsd->fd", activated, masked_grad, preferred_element_type=jnp.float32)
        )
    grad_down_weight = jnp.stack(down_list, axis=0)
    grad_up = jax.vjp(gelu_exact, upward)[1](grad_act)[0].astype(jnp.bfloat16)
    in_list = []
    for expert in range(experts):
        in_list.append(
            jnp.einsum(
                "rsd,rsf->df",
                select_rows(norm_two_full, hot_matrix[:, expert]),
                grad_up,
                preferred_element_type=jnp.float32,
            )
        )
    grad_in_weight = jnp.stack(in_list, axis=0)
    ffn_grads = (grad_in_weight.astype(jnp.bfloat16), grad_down_weight.astype(jnp.bfloat16))
    ffn_grads, grad_up = lax.optimization_barrier((ffn_grads, grad_up))
    ffn_summed = lax.psum(ffn_grads, "dp")
    picked = grad_up
    hot_picked = hot_matrix
    total = jnp.zeros((local_rows * lax.axis_size("mp"), slots, model_width), jnp.float32)
    for expert in range(experts):
        total = total + jnp.einsum(
            "rsf,df->rsd",
            select_rows(picked, hot_picked[:, expert]),
            in_weight[expert],
            preferred_element_type=jnp.float32,
        )
    grad_norm_two = scatter_rows_mp(total)
    second_back = jax.vjp(layer_norm, residual, gain_ffn, shift_ffn)[1]
    grad_from_second, grad_gain_ffn, grad_shift_ffn = second_back(grad_norm_two)
    grad_residual = grad_output + grad_from_second
    grad_attn_full = gather_rows_mp(grad_residual.astype(jnp.bfloat16))
    ffn_partial, grad_attn_full = lax.optimization_barrier((ffn_partial, grad_attn_full))
    output = (residual + scatter_rows_mp(ffn_partial)).astype(jnp.bfloat16)
    grad_out_weight = jnp.einsum(
        "rsk,rsd->kd", head_mix, grad_attn_full, preferred_element_type=jnp.float32
    )
    grad_mix = jnp.einsum(
        "rsd,kd->rsk", grad_attn_full, out_weight, preferred_element_type=jnp.float32
    )
    grad_mix = grad_mix.astype(jnp.bfloat16).reshape(group_rows, slots, heads_local, HD)
    attn_again = jnp.exp(masked_scores() - log_total)
    grad_probs = jnp.einsum(
        "rqhd,rkhd->rhqk", grad_mix, value_part, preferred_element_type=jnp.float32
    )
    grad_scores = attn_again * (
        grad_probs - jnp.sum(grad_probs * attn_again, axis=-1, keepdims=True)
    )
    grad_scores = grad_scores.astype(jnp.bfloat16)
    grad_value = jnp.einsum(
        "rhqk,rqhd->rkhd",
        attn_again.astype(jnp.bfloat16),
        grad_mix,
        preferred_element_type=jnp.float32,
    )
    grad_query = (
        jnp.einsum("rhqk,rkhd->rqhd", grad_scores, key_part, preferred_element_type=jnp.float32)
        * score_scale
    )
    grad_key = (
        jnp.einsum("rhqk,rqhd->rkhd", grad_scores, queries, preferred_element_type=jnp.float32)
        * score_scale
    )
    grad_qkv = (
        jnp.stack([grad_query, grad_key, grad_value], axis=2)
        .astype(jnp.bfloat16)
        .reshape(group_rows, slots, -1)
    )
    grad_qkv_weight = jnp.einsum(
        "rsd,rsk->dk", norm_one_full, grad_qkv, preferred_element_type=jnp.float32
    )
    grad_qkv_weight = grad_qkv_weight.reshape(qkv_weight.shape)
    picked = grad_qkv
    grad_norm_one = scatter_rows_mp(
        jnp.einsum("rsk,dk->rsd", picked, qkv_flat, preferred_element_type=jnp.float32)
    )
    first_back = jax.vjp(layer_norm, token_float, gain_attn, shift_attn)[1]
    grad_from_first, grad_gain_attn, grad_shift_attn = first_back(grad_norm_one)
    grad_tokens = grad_residual + grad_from_first
    norm_grads = butterfly_sum(
        butterfly_sum(
            jnp.stack([grad_gain_attn, grad_shift_attn, grad_gain_ffn, grad_shift_ffn]), "mp"
        ),
        "dp",
    )
    attn_summed = butterfly_allreduce_low((grad_qkv_weight, grad_out_weight), "dp")
    summed = attn_summed + tuple(g.astype(jnp.float32) for g in ffn_summed)
    return (
        output,
        grad_tokens,
        counts,
        summed[0],
        summed[1],
        summed[2],
        summed[3],
        norm_grads[0],
        norm_grads[1],
        norm_grads[2],
        norm_grads[3],
    )


def solution(mesh):
    in_specs = (
        P(("dp", "mp"), None, None),
        P(("dp", "mp"), None, None),
        P("dp", None),
        P("dp", None),
        P("dp"),
        P(None, None, "mp"),
        P("mp", None),
        P(None, None, "mp"),
        P(None, "mp", None),
        P(),
        P(),
        P(),
        P(),
    )
    out_specs = (
        P(("dp", "mp"), None, None),
        P(("dp", "mp"), None, None),
        P(),
        P(None, None, "mp"),
        P("mp", None),
        P(None, None, "mp"),
        P(None, "mp", None),
        P(),
        P(),
        P(),
        P(),
    )

    return jax.shard_map(per_device, mesh=mesh, in_specs=in_specs, out_specs=out_specs, check_vma=False)
```

```python
import jax
import jax.numpy as jnp
from jax import lax
from jax.sharding import PartitionSpec as P


HD = 64


norm_epsilon = 1e-05
masked_fill = -1e30


def layer_norm(values, norm_gain, norm_shift):
    average = jnp.mean(values, axis=-1, keepdims=True)
    centred = values - average
    variance = jnp.mean(centred * centred, axis=-1, keepdims=True)
    return centred * lax.rsqrt(variance + norm_epsilon) * norm_gain + norm_shift


def gelu_exact(values):
    return jax.nn.gelu(values, approximate=False)


def xor_pairs(size, bit):
    return [(i, i ^ bit) for i in range(size)]


def gather_rows_mp(values):
    if lax.axis_size("mp") != 4:
        return lax.all_gather(values, "mp", axis=0, tiled=True)
    index = lax.axis_index("mp")
    chip_y = index // 2
    core = index % 2
    other_y = lax.ppermute(values, "mp", xor_pairs(4, 2))
    pair = jnp.where(
        chip_y == 0, jnp.stack([values, other_y]), jnp.stack([other_y, values])
    )
    other_core = lax.ppermute(pair, "mp", xor_pairs(4, 1))
    quad = jnp.where(
        core == 0, jnp.stack([pair, other_core], axis=1), jnp.stack([other_core, pair], axis=1)
    )
    return quad.reshape((-1,) + values.shape[1:])


def scatter_rows_mp(partial, tie=None):
    if lax.axis_size("mp") != 4:
        result = lax.psum_scatter(
            partial.astype(jnp.bfloat16), "mp", scatter_dimension=0, tiled=True
        ).astype(jnp.float32)
        return result if tie is None else (result, tie)
    index = lax.axis_index("mp")
    chip_y = index // 2
    core = index % 2
    rows = partial.shape[0] // 4
    blocks = partial.reshape((2, 2, rows) + partial.shape[1:])
    keep = lax.dynamic_index_in_dim(blocks, core, axis=1, keepdims=False)
    send = lax.dynamic_index_in_dim(blocks, 1 - core, axis=1, keepdims=False)
    got = lax.ppermute(send.astype(jnp.bfloat16), "mp", xor_pairs(4, 1))
    chip_sum = keep + got.astype(jnp.float32)
    keep_y = lax.dynamic_index_in_dim(chip_sum, chip_y, axis=0, keepdims=False)
    send_y = lax.dynamic_index_in_dim(chip_sum, 1 - chip_y, axis=0, keepdims=False)
    got_y = lax.ppermute(send_y.astype(jnp.bfloat16), "mp", xor_pairs(4, 2))
    if tie is not None:
        tie, got_y = lax.optimization_barrier((tie, got_y))
    result = keep_y + got_y.astype(jnp.float32)
    return result if tie is None else (result, tie)


def butterfly_sum(values, axis):
    size = lax.axis_size(axis)
    if size & (size - 1):
        return lax.psum(values, axis)
    bit = 1
    while bit < size:
        values = jax.tree.map(
            lambda v: v + lax.ppermute(v, axis, xor_pairs(size, bit)), values
        )
        bit *= 2
    return values


def butterfly_allreduce_low(values, axis):
    size = lax.axis_size(axis)
    flat = jnp.concatenate([v.reshape(-1).astype(jnp.float32) for v in values])
    if size & (size - 1) or flat.shape[0] % size:
        summed = lax.psum(flat.astype(jnp.bfloat16), axis)
    else:
        steps = size.bit_length() - 1
        index = lax.axis_index(axis)
        chunk = flat.shape[0] // size
        held = flat.reshape((2,) * steps + (chunk,))
        for step in range(steps):
            bit = 1 << step
            mine = (index // bit) % 2
            last = steps - 1 - step
            keep = lax.dynamic_index_in_dim(held, mine, axis=last, keepdims=False)
            send = lax.dynamic_index_in_dim(held, 1 - mine, axis=last, keepdims=False)
            got = lax.ppermute(send.astype(jnp.bfloat16), axis, xor_pairs(size, bit))
            held = keep + got.astype(jnp.float32)
        held = held.astype(jnp.bfloat16)
        for step in reversed(range(steps)):
            bit = 1 << step
            mine = (index // bit) % 2
            got = lax.ppermute(held, axis, xor_pairs(size, bit))
            place = steps - 1 - step
            held = jnp.where(
                mine == 0, jnp.stack([held, got], axis=place), jnp.stack([got, held], axis=place)
            )
        summed = held.reshape(-1)
    out, start = [], 0
    for v in values:
        out.append(summed[start : start + v.size].reshape(v.shape).astype(jnp.float32))
        start += v.size
    return tuple(out)


def select_rows(values, hot_column):
    return values * hot_column[:, None, None]


def per_device(
    tokens,
    cotangent,
    segment_ids,
    live_mask,
    expert_ids,
    qkv_weight,
    out_weight,
    in_weight,
    down_weight,
    gain_attn,
    shift_attn,
    gain_ffn,
    shift_ffn,
):
    local_rows, slots, model_width = tokens.shape
    experts = in_weight.shape[0]
    heads_local = qkv_weight.shape[2] // HD
    score_scale = HD ** (-0.5)
    first_row = lax.axis_index("mp") * local_rows
    expert_hot = expert_ids[:, None] == jnp.arange(experts)[None, :]
    row_live = jnp.sum(live_mask, axis=1)
    local_counts = jnp.sum(jnp.where(expert_hot, row_live[:, None], 0), axis=0)
    counts = butterfly_sum(local_counts, "dp")
    hot_matrix = expert_hot.astype(jnp.bfloat16)
    token_float = tokens.astype(jnp.float32)
    norm_one = layer_norm(token_float, gain_attn, shift_attn).astype(jnp.bfloat16)
    norm_one_full = gather_rows_mp(norm_one)
    qkv_flat = qkv_weight.reshape(model_width, -1)
    qkv_all = jnp.einsum(
        "rsd,dk->rsk", norm_one_full, qkv_flat, preferred_element_type=jnp.float32
    ).astype(jnp.bfloat16)
    group_rows = qkv_all.shape[0]
    qkv_split = qkv_all.reshape(group_rows, slots, 3, heads_local, HD)
    queries = qkv_split[:, :, 0]
    key_part = qkv_split[:, :, 1]
    value_part = qkv_split[:, :, 2]
    same_caption = segment_ids[:, :, None] == segment_ids[:, None, :]
    diagonal = jnp.arange(slots)[:, None] == jnp.arange(slots)[None, :]
    allowed = (same_caption & ((live_mask[:, None, :] == 1) | diagonal[None]))[:, None]

    def masked_scores():
        raw_scores = (
            jnp.einsum("rqhd,rkhd->rhqk", queries, key_part, preferred_element_type=jnp.float32)
            * score_scale
        )
        return jnp.where(allowed, raw_scores, masked_fill)

    scores = masked_scores()
    row_top = jnp.max(scores, axis=-1, keepdims=True)
    exp_scores = jnp.exp(scores - row_top)
    row_total = jnp.sum(exp_scores, axis=-1, keepdims=True)
    attn_probs = exp_scores / row_total
    log_total = row_top + jnp.log(row_total)
    head_mix = jnp.einsum(
        "rhqk,rkhd->rqhd",
        attn_probs.astype(jnp.bfloat16),
        value_part,
        preferred_element_type=jnp.float32,
    )
    head_mix = head_mix.reshape(group_rows, slots, heads_local * HD).astype(jnp.bfloat16)
    picked = head_mix
    attn_partial = jnp.einsum("rsk,kd->rsd", picked, out_weight, preferred_element_type=jnp.float32)
    count_float = counts.astype(jnp.float32)
    loss_weight = jnp.sum(count_float) / (experts * count_float)
    local_hot = lax.dynamic_slice_in_dim(expert_hot, first_row, local_rows, 0)
    row_weight = jnp.sum(jnp.where(local_hot, loss_weight[None, :], 0.0), axis=1)
    live_local = lax.dynamic_slice_in_dim(live_mask, first_row, local_rows, 0)
    grad_output = (
        cotangent.astype(jnp.float32)
        * live_local[:, :, None].astype(jnp.float32)
        * row_weight[:, None, None]
    )
    grad_ffn_full = gather_rows_mp(grad_output.astype(jnp.bfloat16))
    grad_ffn_full, attn_partial = lax.optimization_barrier((grad_ffn_full, attn_partial))
    attn_local = scatter_rows_mp(attn_partial)
    residual = token_float + attn_local
    norm_two = layer_norm(residual, gain_ffn, shift_ffn).astype(jnp.bfloat16)
    norm_two_full = gather_rows_mp(norm_two)
    upward = jnp.zeros((group_rows, slots, in_weight.shape[2]), jnp.float32)
    for expert in range(experts):
        upward = upward + jnp.einsum(
            "rsd,df->rsf",
            select_rows(norm_two_full, hot_matrix[:, expert]),
            in_weight[expert],
            preferred_element_type=jnp.float32,
        )
    activated = gelu_exact(upward).astype(jnp.bfloat16)
    picked = activated
    hot_picked = hot_matrix
    total = jnp.zeros((local_rows * lax.axis_size("mp"), slots, model_width), jnp.float32)
    for ffn_expert in range(experts):
        total = total + jnp.einsum(
            "rsf,fd->rsd",
            select_rows(picked, hot_picked[:, ffn_expert]),
            down_weight[ffn_expert],
            preferred_element_type=jnp.float32,
        )
    ffn_partial = total
    grad_act = jnp.zeros(upward.shape, jnp.float32)
    down_list = []
    for expert in range(experts):
        masked_grad = select_rows(grad_ffn_full, hot_matrix[:, expert])
        grad_act = grad_act + jnp.einsum(
            "rsd,fd->rsf", masked_grad, down_weight[expert], preferred_element_type=jnp.float32
        )
        down_list.append(
            jnp.einsum("rsf,rsd->fd", activated, masked_grad, preferred_element_type=jnp.float32)
        )
    grad_down_weight = jnp.stack(down_list, axis=0)
    grad_up = jax.vjp(gelu_exact, upward)[1](grad_act)[0].astype(jnp.bfloat16)
    in_list = []
    for expert in range(experts):
        in_list.append(
            jnp.einsum(
                "rsd,rsf->df",
                select_rows(norm_two_full, hot_matrix[:, expert]),
                grad_up,
                preferred_element_type=jnp.float32,
            )
        )
    grad_in_weight = jnp.stack(in_list, axis=0)
    ffn_grads = (grad_in_weight.astype(jnp.bfloat16), grad_down_weight.astype(jnp.bfloat16))
    ffn_grads, grad_up = lax.optimization_barrier((ffn_grads, grad_up))
    ffn_summed = lax.psum(ffn_grads, "dp")
    picked = grad_up
    hot_picked = hot_matrix
    total = jnp.zeros((local_rows * lax.axis_size("mp"), slots, model_width), jnp.float32)
    for expert in range(experts):
        total = total + jnp.einsum(
            "rsf,df->rsd",
            select_rows(picked, hot_picked[:, expert]),
            in_weight[expert],
            preferred_element_type=jnp.float32,
        )
    grad_norm_two = scatter_rows_mp(total)
    second_back = jax.vjp(layer_norm, residual, gain_ffn, shift_ffn)[1]
    grad_from_second, grad_gain_ffn, grad_shift_ffn = second_back(grad_norm_two)
    grad_residual = grad_output + grad_from_second
    grad_attn_full = gather_rows_mp(grad_residual.astype(jnp.bfloat16))
    ffn_partial, grad_attn_full = lax.optimization_barrier((ffn_partial, grad_attn_full))
    output = (residual + scatter_rows_mp(ffn_partial)).astype(jnp.bfloat16)
    grad_out_weight = jnp.einsum(
        "rsk,rsd->kd", head_mix, grad_attn_full, preferred_element_type=jnp.float32
    )
    grad_mix = jnp.einsum(
        "rsd,kd->rsk", grad_attn_full, out_weight, preferred_element_type=jnp.float32
    )
    grad_mix = grad_mix.astype(jnp.bfloat16).reshape(group_rows, slots, heads_local, HD)
    attn_again = jnp.exp(masked_scores() - log_total)
    grad_probs = jnp.einsum(
        "rqhd,rkhd->rhqk", grad_mix, value_part, preferred_element_type=jnp.float32
    )
    grad_scores = attn_again * (
        grad_probs - jnp.sum(grad_probs * attn_again, axis=-1, keepdims=True)
    )
    grad_scores = grad_scores.astype(jnp.bfloat16)
    grad_value = jnp.einsum(
        "rhqk,rqhd->rkhd",
        attn_again.astype(jnp.bfloat16),
        grad_mix,
        preferred_element_type=jnp.float32,
    )
    grad_query = (
        jnp.einsum("rhqk,rkhd->rqhd", grad_scores, key_part, preferred_element_type=jnp.float32)
        * score_scale
    )
    grad_key = (
        jnp.einsum("rhqk,rqhd->rkhd", grad_scores, queries, preferred_element_type=jnp.float32)
        * score_scale
    )
    grad_qkv = (
        jnp.stack([grad_query, grad_key, grad_value], axis=2)
        .astype(jnp.bfloat16)
        .reshape(group_rows, slots, -1)
    )
    grad_qkv_weight = jnp.einsum(
        "rsd,rsk->dk", norm_one_full, grad_qkv, preferred_element_type=jnp.float32
    )
    grad_qkv_weight = grad_qkv_weight.reshape(qkv_weight.shape)
    picked = grad_qkv
    grad_norm_one = scatter_rows_mp(
        jnp.einsum("rsk,dk->rsd", picked, qkv_flat, preferred_element_type=jnp.float32)
    )
    first_back = jax.vjp(layer_norm, token_float, gain_attn, shift_attn)[1]
    grad_from_first, grad_gain_attn, grad_shift_attn = first_back(grad_norm_one)
    grad_tokens = grad_residual + grad_from_first
    norm_grads = butterfly_sum(
        butterfly_sum(
            jnp.stack([grad_gain_attn, grad_shift_attn, grad_gain_ffn, grad_shift_ffn]), "mp"
        ),
        "dp",
    )
    attn_grads, ffn_summed = lax.optimization_barrier(
        ((grad_qkv_weight, grad_out_weight), ffn_summed)
    )
    attn_summed = butterfly_allreduce_low(attn_grads, "dp")
    summed = attn_summed + tuple(g.astype(jnp.float32) for g in ffn_summed)
    return (
        output,
        grad_tokens,
        counts,
        summed[0],
        summed[1],
        summed[2],
        summed[3],
        norm_grads[0],
        norm_grads[1],
        norm_grads[2],
        norm_grads[3],
    )


def solution(mesh):
    in_specs = (
        P(("dp", "mp"), None, None),
        P(("dp", "mp"), None, None),
        P("dp", None),
        P("dp", None),
        P("dp"),
        P(None, None, "mp"),
        P("mp", None),
        P(None, None, "mp"),
        P(None, "mp", None),
        P(),
        P(),
        P(),
        P(),
    )
    out_specs = (
        P(("dp", "mp"), None, None),
        P(("dp", "mp"), None, None),
        P(),
        P(None, None, "mp"),
        P("mp", None),
        P(None, None, "mp"),
        P(None, "mp", None),
        P(),
        P(),
        P(),
        P(),
    )

    return jax.shard_map(per_device, mesh=mesh, in_specs=in_specs, out_specs=out_specs, check_vma=False)
```
